256 devices in a mesh: expert: 8 (over z_lo, core), tensor: 32 (over z_hi, x, y).
Axes of the slice: x: 4, y: 4, z: 8 (z_hi: 2, z_lo: 4; z = z_hi * 4 + z_lo), core: 2. Of those that a mesh axis runs over, the one named last changes fastest.
Arguments:
- tokens: bfloat16 [2048, 6144], P('expert', 'tensor'), may hold values from -6 to 6
- router_weight: bfloat16 [6144, 8], replicated, may hold values from -0.078125 to 0.078125
- expert_ids: int32 [2048, 2], P('expert'), may hold values from 0 to 7, all different within a row
- w_gate: bfloat16 [8, 6144, 8192], P('expert', None, 'tensor'), may hold values from -0.078125 to 0.078125
- w_up: bfloat16 [8, 6144, 8192], P('expert', None, 'tensor'), may hold values from -0.078125 to 0.078125
- w_down: bfloat16 [8, 8192, 6144], P('expert', 'tensor'), may hold values from -0.125 to 0.125
Outputs:
- moe_out: bfloat16 [2048, 6144], P('expert', 'tensor')
The draws below stay inside these ranges and needn't reach their ends.
Inputs may be any that keep to these rules, and one draw needn't show every extreme that they name: `expert_ids`: each row names 2 different experts, and every expert is named by some row.
All inputs are finite; a program needn't handle non-finite values.
Results may differ from the reference program's by a relative error of at most 0.03.
Values may be sent and summed in bfloat16 or wider, within the bound.
No kernel may reach another device: no remote copies, remote signals or barrier semaphores. Data moves between devices by JAX's collectives and lax.ppermute only.
A program may use at most 64 MiB of HBM per device.

```python
import jax
import jax.numpy as jnp
from jax import lax

D = 6144
FF = 8192
TOP = 2
TOK_DEV = 256
EXPERTS = 8
CAP = 80
TOKENS = 2048
FF_DEV = 256
N_EXPERT = 8
N_TENSOR = 32


def strengthened(values, own_key, source, target, parts, factor):
    def block_of(dim):
        return (jnp.arange(values.shape[dim]) // (values.shape[dim] // parts)).reshape((-1,) + (1,) * (values.ndim - 1 - dim))

    first = jax.random.permutation(own_key, parts)[block_of(target)]
    far = (block_of(target) + parts // 2) % parts
    return jnp.where((block_of(source) == first) | (block_of(source) == far), factor * values, values)


def steps_of(key, dims, cuts, low, largest):
    def one(dim, parts):
        heights = jax.random.uniform(jax.random.fold_in(jax.random.fold_in(key, 6), dim), (parts,), jnp.float32, low / len(cuts), largest / len(cuts))
        return jnp.repeat(jnp.exp(heights), dims[dim] // parts).reshape((-1,) + (1,) * (len(dims) - dim - 1))

    factor_of = one(*cuts[0])
    for cut in cuts[1:]:
        factor_of = factor_of * one(*cut)
    return factor_of


def different_ones(key, rows, amount, top, lift):
    order = jax.random.permutation(jax.random.fold_in(key, 1), amount)
    favour = order
    for power in range(3):
        favour = favour * favour // amount
    favour = favour * lift // amount
    tickets = jax.random.randint(jax.random.fold_in(key, 2), (rows, amount), 0, 4096) + favour
    sure = jax.random.permutation(jax.random.fold_in(key, 3), rows)[jnp.arange(amount) % rows]
    tickets = jnp.where(jnp.arange(rows)[:, None] == sure[None, :], 1 << 14, tickets)
    merit = tickets * amount + jnp.arange(amount)
    return lax.top_k(merit.astype(jnp.int32), top)[1].astype(jnp.int32)


def noise(own_key, extent, deviation, limit, shards=(), kind=jnp.bfloat16):
    drawn = jax.random.normal(own_key, extent, jnp.float32) * deviation
    if len(shards) > 0:
        drawn = steps_of(own_key, extent, shards, -0.22, 0.18) * drawn
    return jnp.clip(drawn, min=-limit, max=limit).astype(kind)


def noise_with(stream_key, extent, spread, bound, shards, heavy, kind=jnp.bfloat16):
    entries = spread * jax.random.normal(stream_key, extent, jnp.float32)
    if shards:
        entries = entries * steps_of(stream_key, extent, shards, -0.22, 0.18)
    return jnp.clip(strengthened(entries, jax.random.fold_in(stream_key, 3), *heavy), -bound, bound).astype(kind)


def setup_inputs(seed: int = 0) -> dict:
    key_list = jax.random.split(jax.random.key(seed), 7)
    tokens = noise(key_list[0], (TOKENS, D), 1.0, 6.0, ((0, 8), (1, 32)))
    router_weight = noise(key_list[1], (D, EXPERTS), D ** -0.5, 0.078125)
    expert_ids = different_ones(key_list[2], TOKENS, EXPERTS, TOP, 2048)
    w_gate = noise(key_list[3], (EXPERTS, D, FF), D ** -0.5, 0.078125, ((0, 8), (2, 32)))
    w_up = noise(key_list[4], (EXPERTS, D, FF), D ** -0.5, 0.078125, ((0, 8), (2, 32)))
    w_down = noise_with(key_list[5], (EXPERTS, FF, D), FF ** -0.5, 0.125, ((0, 8), (1, 32)), (1, 2, 32, 2.75))
    return dict(tokens=tokens, router_weight=router_weight, expert_ids=expert_ids, w_gate=w_gate, w_up=w_up, w_down=w_down)


def reference(tokens, router_weight, expert_ids, w_gate, w_up, w_down):
    logits = jnp.dot(tokens, router_weight, preferred_element_type=jnp.float32)
    chosen = jnp.take_along_axis(logits, expert_ids, axis=1)
    weight = jax.nn.sigmoid(chosen - chosen[:, ::-1]).astype(jnp.bfloat16)
    weight = lax.optimization_barrier(weight).astype(jnp.float32)
    group_ids = expert_ids.reshape(N_EXPERT, TOK_DEV * TOP)
    expert_hot = (group_ids[..., None] == jnp.arange(EXPERTS, dtype=jnp.int32)).astype(jnp.int32)
    earlier = jnp.cumsum(expert_hot, axis=1) - expert_hot
    slot = jnp.sum(earlier * expert_hot, axis=2).astype(jnp.int32)
    kept = slot < CAP
    target = jnp.where(kept, group_ids * CAP + slot, EXPERTS * CAP).astype(jnp.int32)
    grouped = jnp.repeat(tokens.reshape(N_EXPERT, TOK_DEV, D), TOP, axis=1)

    def fill(where, rows):
        empty = jnp.zeros((EXPERTS * CAP + 1, D), jnp.bfloat16)
        return empty.at[where].set(rows)[:-1]

    bucket = jax.vmap(fill)(target, grouped).reshape(N_EXPERT, EXPERTS, CAP, D)
    bucket = jnp.transpose(bucket, (1, 0, 2, 3)).reshape(EXPERTS, N_EXPERT * CAP, D)

    def one_expert(items):
        rows, gate_w, up_w, down_w = items
        gate = jnp.dot(rows, gate_w, preferred_element_type=jnp.float32)
        upper = jnp.dot(rows, up_w, preferred_element_type=jnp.float32)
        hidden = (jax.nn.silu(gate) * upper).astype(jnp.bfloat16)
        blocks = jnp.transpose(hidden.reshape(N_EXPERT * CAP, N_TENSOR, FF_DEV), (1, 0, 2))
        down_blocks = down_w.reshape(N_TENSOR, FF_DEV, D)

        def add(total, pair):
            part = jnp.dot(pair[0], pair[1], preferred_element_type=jnp.float32).astype(jnp.bfloat16)
            return total + lax.optimization_barrier(part).astype(jnp.float32), None

        total, _ = lax.scan(add, jnp.zeros((N_EXPERT * CAP, D), jnp.float32), (blocks, down_blocks))
        return total.astype(jnp.bfloat16).reshape(N_EXPERT, CAP, D)

    expert_out = lax.map(one_expert, (bucket, w_gate, w_up, w_down))
    group_index = jnp.arange(N_EXPERT, dtype=jnp.int32)[:, None]
    picked = expert_out[group_ids, group_index, jnp.minimum(slot, CAP - 1)].astype(jnp.float32)
    picked = jnp.where(kept[..., None], picked, 0.0).reshape(N_EXPERT, TOK_DEV, TOP, D)
    scaled = picked * weight.reshape(N_EXPERT, TOK_DEV, TOP)[..., None]
    return jnp.sum(scaled, axis=2).reshape(TOKENS, D).astype(jnp.bfloat16)
```

```python
import jax
import jax.numpy as jnp
from jax import lax
from jax.sharding import Mesh
from jax.sharding import PartitionSpec as P

EXPERT = "expert"
ZH, GX, GY = "zh", "x", "y"
TENSOR = (ZH, GX, GY)


def body(tokens, router_weight, expert_ids, w_gate, w_up, w_down):
    tok_rows, part_width = tokens.shape
    top_count = expert_ids.shape[1]
    n_experts = lax.axis_size(EXPERT)
    n_hi = lax.axis_size(ZH)
    n_plane = lax.axis_size(GX) * lax.axis_size(GY)
    capacity = 5 * tok_rows * top_count // (4 * n_experts)
    slots_all = n_experts * capacity
    d_model = router_weight.shape[0]
    my_expert = lax.axis_index(EXPERT)

    flat_ids = expert_ids.reshape(-1)
    picks = tok_rows * top_count
    expert_hot = (flat_ids[:, None] == jnp.arange(n_experts, dtype=jnp.int32)[None, :]).astype(jnp.float32)
    lower = (jnp.arange(picks)[:, None] > jnp.arange(picks)[None, :]).astype(jnp.float32)
    before = jnp.dot(lower, expert_hot, precision=lax.Precision.HIGHEST)
    slot_pos = jnp.sum(before * expert_hot, axis=1).astype(jnp.int32)
    kept = slot_pos < capacity
    target = flat_ids * capacity + slot_pos
    placed = (target[:, None] == jnp.arange(slots_all, dtype=jnp.int32)[None, :]) & kept[:, None]
    placed = placed.reshape(tok_rows, top_count, slots_all).astype(jnp.float32)
    dispatch = jnp.sum(placed, axis=1).astype(jnp.bfloat16)
    other_id = jnp.flip(expert_ids, axis=1).astype(jnp.float32)
    other_of_slot = jnp.sum(placed * other_id[:, :, None], axis=(0, 1))

    bucket_t = lax.dot_general(
        tokens, dispatch, (((0,), (0,)), ((), ())), preferred_element_type=jnp.float32
    ).astype(jnp.bfloat16)
    meta = jnp.broadcast_to(other_of_slot.astype(jnp.bfloat16)[None, :], (8, slots_all))
    payload = jnp.concatenate([bucket_t, meta], axis=0)
    arrived = lax.all_to_all(payload, EXPERT, split_axis=1, concat_axis=1, tiled=True)
    rows_t = arrived[:part_width]
    other_here = arrived[part_width].astype(jnp.int32)

    rows_t = lax.all_gather(rows_t, ZH, axis=0, tiled=True)
    rows_t = lax.all_gather(rows_t, (GX, GY), axis=0, tiled=True)

    def plane_major(w):
        tail = w.shape[1:]
        w = w.reshape((n_hi, n_plane, part_width) + tail)
        return jnp.swapaxes(w, 0, 1).reshape((d_model,) + tail)

    contract_first = (((0,), (0,)), ((), ()))
    logits = lax.dot_general(rows_t, plane_major(router_weight), contract_first, preferred_element_type=jnp.float32)
    expert_col = jnp.arange(n_experts, dtype=jnp.int32)[None, :]
    own_logit = jnp.sum(jnp.where(expert_col == my_expert, logits, 0.0), axis=1)
    other_logit = jnp.sum(jnp.where(expert_col == other_here[:, None], logits, 0.0), axis=1)
    weight = jax.nn.sigmoid(own_logit - other_logit).astype(jnp.bfloat16).astype(jnp.float32)

    gate = lax.dot_general(rows_t, plane_major(w_gate[0]), contract_first, preferred_element_type=jnp.float32)
    upper = lax.dot_general(rows_t, plane_major(w_up[0]), contract_first, preferred_element_type=jnp.float32)
    hidden = (jax.nn.silu(gate) * upper * weight[:, None]).astype(jnp.bfloat16)

    down = w_down[0]
    partial = lax.dot_general(down, hidden, (((0,), (1,)), ((), ())), preferred_element_type=jnp.float32)
    partial = plane_major(partial.astype(jnp.bfloat16))
    summed = lax.psum_scatter(partial, (GX, GY), scatter_dimension=0, tiled=True)
    summed = lax.psum_scatter(summed, ZH, scatter_dimension=0, tiled=True)
    returned = lax.all_to_all(summed, EXPERT, split_axis=1, concat_axis=1, tiled=True)

    combine = dispatch
    mixed = lax.dot_general(combine, returned, (((1,), (1,)), ((), ())), preferred_element_type=jnp.float32)
    return mixed.astype(jnp.bfloat16)


def solution(mesh):
    n_expert, n_tensor = mesh.devices.shape
    fine = Mesh(mesh.devices.reshape(n_expert, 2, 4, n_tensor // 8), (EXPERT, ZH, GX, GY))
    in_specs = (
        P(EXPERT, TENSOR),
        P(),
        P(EXPERT, None),
        P(EXPERT, None, TENSOR),
        P(EXPERT, None, TENSOR),
        P(EXPERT, TENSOR, None),
    )
    out_specs = P(EXPERT, TENSOR)
    return jax.shard_map(body, mesh=fine, in_specs=in_specs, out_specs=out_specs, check_vma=False)
```

```python
import jax
import jax.numpy as jnp
from jax import lax
from jax.sharding import Mesh
from jax.sharding import PartitionSpec as P

EXPERT = "expert"
ZH, GX, GY = "zh", "x", "y"
TENSOR = (ZH, GX, GY)
N_CHUNKS = 2


def body(tokens, router_weight, expert_ids, w_gate, w_up, w_down):
    tok_rows, part_width = tokens.shape
    top_count = expert_ids.shape[1]
    n_experts = lax.axis_size(EXPERT)
    n_hi = lax.axis_size(ZH)
    n_plane = lax.axis_size(GX) * lax.axis_size(GY)
    capacity = 5 * tok_rows * top_count // (4 * n_experts)
    slots_all = n_experts * capacity
    d_model = router_weight.shape[0]
    my_expert = lax.axis_index(EXPERT)

    flat_ids = expert_ids.reshape(-1)
    picks = tok_rows * top_count
    expert_hot = (flat_ids[:, None] == jnp.arange(n_experts, dtype=jnp.int32)[None, :]).astype(jnp.float32)
    lower = (jnp.arange(picks)[:, None] > jnp.arange(picks)[None, :]).astype(jnp.float32)
    before = jnp.dot(lower, expert_hot, precision=lax.Precision.HIGHEST)
    slot_pos = jnp.sum(before * expert_hot, axis=1).astype(jnp.int32)
    kept = slot_pos < capacity
    target = flat_ids * capacity + slot_pos
    placed = (target[:, None] == jnp.arange(slots_all, dtype=jnp.int32)[None, :]) & kept[:, None]
    placed = placed.reshape(tok_rows, top_count, slots_all).astype(jnp.float32)
    dispatch = jnp.sum(placed, axis=1).astype(jnp.bfloat16)
    other_id = jnp.flip(expert_ids, axis=1).astype(jnp.float32)
    other_of_slot = jnp.sum(placed * other_id[:, :, None], axis=(0, 1))

    bucket_t = lax.dot_general(
        tokens, dispatch, (((0,), (0,)), ((), ())), preferred_element_type=jnp.float32
    ).astype(jnp.bfloat16)
    meta = jnp.broadcast_to(other_of_slot.astype(jnp.bfloat16)[None, :], (8, slots_all))
    payload = jnp.concatenate([bucket_t, meta], axis=0)
    rows_in = payload.shape[0]
    payload = jnp.swapaxes(payload.reshape(rows_in, n_experts, capacity), 0, 1)
    payload = jnp.broadcast_to(payload[:, None], (n_experts, n_hi, rows_in, capacity))
    payload = payload.reshape(n_experts * n_hi, rows_in, capacity)
    got = lax.all_to_all(payload, (EXPERT, ZH), 0, 0, tiled=True)
    got = got.reshape(n_experts, n_hi, rows_in, capacity)
    other_here = got[:, 0, part_width, :].reshape(slots_all).astype(jnp.int32)
    rows_t = jnp.transpose(got[:, :, :part_width, :], (1, 2, 0, 3)).reshape(n_hi * part_width, slots_all)

    def plane_major(w, axis):
        shape = w.shape
        w = w.reshape(shape[:axis] + (n_hi, n_plane, part_width) + shape[axis + 1 :])
        return jnp.swapaxes(w, axis, axis + 1).reshape(shape)

    router_pm = plane_major(router_weight, 0)
    gate_pm = plane_major(w_gate[0], 0)
    up_pm = plane_major(w_up[0], 0)
    down_pm = plane_major(w_down[0], 1)
    contract_first = (((0,), (0,)), ((), ()))
    expert_col = jnp.arange(n_experts, dtype=jnp.int32)[None, :]

    chunk = slots_all // N_CHUNKS
    sums = []
    ahead = None
    pending = None
    for c in range(N_CHUNKS):
        part = rows_t[:, c * chunk : (c + 1) * chunk]
        if ahead is not None:
            part, _ = lax.optimization_barrier((part, ahead))
        full = lax.all_gather(part, (GX, GY), axis=0, tiled=True)
        ahead = full
        if pending is not None:
            full, pending = lax.optimization_barrier((full, pending))
            sums.append(lax.psum_scatter(pending, (GX, GY), scatter_dimension=1, tiled=True))
        logits = lax.dot_general(full, router_pm, contract_first, preferred_element_type=jnp.float32)
        other = other_here[c * chunk : (c + 1) * chunk]
        own_logit = jnp.sum(jnp.where(expert_col == my_expert, logits, 0.0), axis=1)
        other_logit = jnp.sum(jnp.where(expert_col == other[:, None], logits, 0.0), axis=1)
        weight = jax.nn.sigmoid(own_logit - other_logit).astype(jnp.bfloat16).astype(jnp.float32)
        gate = lax.dot_general(full, gate_pm, contract_first, preferred_element_type=jnp.float32)
        upper = lax.dot_general(full, up_pm, contract_first, preferred_element_type=jnp.float32)
        hidden = (jax.nn.silu(gate) * upper * weight[:, None]).astype(jnp.bfloat16)
        pending = jnp.dot(hidden, down_pm, preferred_element_type=jnp.float32).astype(jnp.bfloat16)
    sums.append(lax.psum_scatter(pending, (GX, GY), scatter_dimension=1, tiled=True))
    summed = jnp.concatenate(sums, axis=0)

    back = summed.reshape(n_experts, capacity, n_hi, part_width)
    back = jnp.swapaxes(back, 1, 2).reshape(n_experts * n_hi, capacity, part_width)
    got = lax.all_to_all(back, (EXPERT, ZH), 0, 0, tiled=True)
    got = got.reshape(n_experts, n_hi, capacity, part_width).astype(jnp.float32)
    returned = jnp.sum(got, axis=1).astype(jnp.bfloat16).reshape(slots_all, part_width)

    combine = dispatch
    mixed = jnp.dot(combine, returned, preferred_element_type=jnp.float32)
    return mixed.astype(jnp.bfloat16)


def solution(mesh):
    n_expert, n_tensor = mesh.devices.shape
    fine = Mesh(mesh.devices.reshape(n_expert, 2, 4, n_tensor // 8), (EXPERT, ZH, GX, GY))
    in_specs = (
        P(EXPERT, TENSOR),
        P(),
        P(EXPERT, None),
        P(EXPERT, None, TENSOR),
        P(EXPERT, None, TENSOR),
        P(EXPERT, TENSOR, None),
    )
    out_specs = P(EXPERT, TENSOR)
    return jax.shard_map(body, mesh=fine, in_specs=in_specs, out_specs=out_specs, check_vma=False)
```

```python
import jax
import jax.numpy as jnp
from jax import lax
from jax.sharding import Mesh
from jax.sharding import PartitionSpec as P

EXPERT = "expert"
ZH, GX, GY = "zh", "x", "y"
TENSOR = (ZH, GX, GY)


def body(tokens, router_weight, expert_ids, w_gate, w_up, w_down):
    tok_rows, part_width = tokens.shape
    top_count = expert_ids.shape[1]
    n_experts = lax.axis_size(EXPERT)
    n_hi = lax.axis_size(ZH)
    n_plane = lax.axis_size(GX) * lax.axis_size(GY)
    capacity = 5 * tok_rows * top_count // (4 * n_experts)
    slots_all = n_experts * capacity
    d_model = router_weight.shape[0]
    my_expert = lax.axis_index(EXPERT)

    flat_ids = expert_ids.reshape(-1)
    picks = tok_rows * top_count
    expert_hot = (flat_ids[:, None] == jnp.arange(n_experts, dtype=jnp.int32)[None, :]).astype(jnp.float32)
    lower = (jnp.arange(picks)[:, None] > jnp.arange(picks)[None, :]).astype(jnp.float32)
    before = jnp.dot(lower, expert_hot, precision=lax.Precision.HIGHEST)
    slot_pos = jnp.sum(before * expert_hot, axis=1).astype(jnp.int32)
    kept = slot_pos < capacity
    target = flat_ids * capacity + slot_pos
    placed = (target[:, None] == jnp.arange(slots_all, dtype=jnp.int32)[None, :]) & kept[:, None]
    placed = placed.reshape(tok_rows, top_count, slots_all).astype(jnp.float32)
    dispatch = jnp.sum(placed, axis=1).astype(jnp.bfloat16)
    other_id = jnp.flip(expert_ids, axis=1).astype(jnp.float32)
    other_of_slot = jnp.sum(placed * other_id[:, :, None], axis=(0, 1))

    bucket_t = lax.dot_general(
        tokens, dispatch, (((0,), (0,)), ((), ())), preferred_element_type=jnp.float32
    ).astype(jnp.bfloat16)
    meta = jnp.broadcast_to(other_of_slot.astype(jnp.bfloat16)[None, :], (8, slots_all))
    payload = jnp.concatenate([bucket_t, meta], axis=0)
    rows_in = payload.shape[0]
    payload = jnp.swapaxes(payload.reshape(rows_in, n_experts, capacity), 0, 1)
    payload = jnp.broadcast_to(payload[:, None], (n_experts, n_hi, rows_in, capacity))
    payload = payload.reshape(n_experts * n_hi, rows_in, capacity)
    got = lax.all_to_all(payload, (EXPERT, ZH), 0, 0, tiled=True)
    got = got.reshape(n_experts, n_hi, rows_in, capacity)
    other_here = got[:, 0, part_width, :].reshape(slots_all).astype(jnp.int32)
    rows_t = jnp.transpose(got[:, :, :part_width, :], (1, 2, 0, 3)).reshape(n_hi * part_width, slots_all)

    def plane_major(w, axis):
        shape = w.shape
        w = w.reshape(shape[:axis] + (n_hi, n_plane, part_width) + shape[axis + 1 :])
        return jnp.swapaxes(w, axis, axis + 1).reshape(shape)

    router_pm = plane_major(router_weight, 0)
    gate_pm = plane_major(w_gate[0], 0)
    up_pm = plane_major(w_up[0], 0)
    down_pm = plane_major(w_down[0], 1)
    contract_first = (((0,), (0,)), ((), ()))
    expert_col = jnp.arange(n_experts, dtype=jnp.int32)[None, :]

    full = lax.all_gather(rows_t, (GX, GY), axis=0, tiled=True)
    logits = lax.dot_general(full, router_pm, contract_first, preferred_element_type=jnp.float32)
    own_logit = jnp.sum(jnp.where(expert_col == my_expert, logits, 0.0), axis=1)
    other_logit = jnp.sum(jnp.where(expert_col == other_here[:, None], logits, 0.0), axis=1)
    weight = jax.nn.sigmoid(own_logit - other_logit).astype(jnp.bfloat16).astype(jnp.float32)
    gate = lax.dot_general(full, gate_pm, contract_first, preferred_element_type=jnp.float32)
    upper = lax.dot_general(full, up_pm, contract_first, preferred_element_type=jnp.float32)
    hidden = (jax.nn.silu(gate) * upper * weight[:, None]).astype(jnp.bfloat16)
    partial = jnp.dot(hidden, down_pm, preferred_element_type=jnp.float32).astype(jnp.bfloat16)
    summed = lax.psum_scatter(partial, (GX, GY), scatter_dimension=1, tiled=True)

    back = summed.reshape(n_experts, capacity, n_hi, part_width)
    back = jnp.swapaxes(back, 1, 2).reshape(n_experts * n_hi, capacity, part_width)
    got = lax.all_to_all(back, (EXPERT, ZH), 0, 0, tiled=True)
    got = got.reshape(n_experts, n_hi, capacity, part_width).astype(jnp.float32)
    returned = jnp.sum(got, axis=1).astype(jnp.bfloat16).reshape(slots_all, part_width)

    combine = dispatch
    mixed = jnp.dot(combine, returned, preferred_element_type=jnp.float32)
    return mixed.astype(jnp.bfloat16)


def solution(mesh):
    n_expert, n_tensor = mesh.devices.shape
    fine = Mesh(mesh.devices.reshape(n_expert, 2, 4, n_tensor // 8), (EXPERT, ZH, GX, GY))
    in_specs = (
        P(EXPERT, TENSOR),
        P(),
        P(EXPERT, None),
        P(EXPERT, None, TENSOR),
        P(EXPERT, None, TENSOR),
        P(EXPERT, TENSOR, None),
    )
    out_specs = P(EXPERT, TENSOR)
    return jax.shard_map(body, mesh=fine, in_specs=in_specs, out_specs=out_specs, check_vma=False)
```

```python
import jax
import jax.numpy as jnp
from jax import lax
from jax.experimental import pallas as pl
from jax.sharding import Mesh
from jax.sharding import PartitionSpec as P

EXPERT = "expert"
ZH, GX, GY = "zh", "x", "y"
TENSOR = (ZH, GX, GY)


def _down_kernel(a_ref, b_ref, o_ref):
    o_ref[...] = jnp.dot(a_ref[...], b_ref[...], preferred_element_type=jnp.float32).astype(o_ref.dtype)


def down_project(down_t, hidden_t):
    d_rows, ff = down_t.shape
    rows = hidden_t.shape[1]
    block = 768
    return pl.pallas_call(
        _down_kernel,
        grid=(d_rows // block,),
        in_specs=[pl.BlockSpec((block, ff), lambda i: (i, 0)), pl.BlockSpec((ff, rows), lambda i: (0, 0))],
        out_specs=pl.BlockSpec((block, rows), lambda i: (i, 0)),
        out_shape=jax.ShapeDtypeStruct((d_rows, rows), jnp.bfloat16),
    )(down_t, hidden_t)


def body(tokens, router_weight, expert_ids, w_gate, w_up, w_down):
    tok_rows, part_width = tokens.shape
    top_count = expert_ids.shape[1]
    n_experts = lax.axis_size(EXPERT)
    n_hi = lax.axis_size(ZH)
    n_plane = lax.axis_size(GX) * lax.axis_size(GY)
    capacity = 5 * tok_rows * top_count // (4 * n_experts)
    slots_all = n_experts * capacity
    d_model = router_weight.shape[0]
    my_expert = lax.axis_index(EXPERT)

    flat_ids = expert_ids.reshape(-1)
    picks = tok_rows * top_count
    expert_hot = (flat_ids[:, None] == jnp.arange(n_experts, dtype=jnp.int32)[None, :]).astype(jnp.float32)
    lower = (jnp.arange(picks)[:, None] > jnp.arange(picks)[None, :]).astype(jnp.float32)
    before = jnp.dot(lower, expert_hot, precision=lax.Precision.HIGHEST)
    slot_pos = jnp.sum(before * expert_hot, axis=1).astype(jnp.int32)
    kept = slot_pos < capacity
    target = flat_ids * capacity + slot_pos
    placed = (target[:, None] == jnp.arange(slots_all, dtype=jnp.int32)[None, :]) & kept[:, None]
    placed = placed.reshape(tok_rows, top_count, slots_all).astype(jnp.float32)
    dispatch = jnp.sum(placed, axis=1).astype(jnp.bfloat16)
    other_id = jnp.flip(expert_ids, axis=1).astype(jnp.float32)
    other_of_slot = jnp.sum(placed * other_id[:, :, None], axis=(0, 1))

    bucket_t = lax.dot_general(
        tokens, dispatch, (((0,), (0,)), ((), ())), preferred_element_type=jnp.float32
    ).astype(jnp.bfloat16)
    meta = jnp.broadcast_to(other_of_slot.astype(jnp.bfloat16)[None, :], (8, slots_all))
    payload = jnp.concatenate([bucket_t, meta], axis=0)
    rows_in = payload.shape[0]
    payload = jnp.swapaxes(payload.reshape(rows_in, n_experts, capacity), 0, 1)
    payload = jnp.broadcast_to(payload[:, None], (n_experts, n_hi, rows_in, capacity))
    payload = payload.reshape(n_experts * n_hi, rows_in, capacity)
    got = lax.all_to_all(payload, (EXPERT, ZH), 0, 0, tiled=True)
    got = got.reshape(n_experts, n_hi, rows_in, capacity)
    other_here = got[:, 0, part_width, :].reshape(slots_all).astype(jnp.int32)
    rows_t = jnp.transpose(got[:, :, :part_width, :], (1, 2, 0, 3)).reshape(n_hi * part_width, slots_all)

    def plane_major(w, axis):
        shape = w.shape
        w = w.reshape(shape[:axis] + (n_hi, n_plane, part_width) + shape[axis + 1 :])
        return jnp.swapaxes(w, axis, axis + 1).reshape(shape)

    ff_dev = w_gate.shape[2]
    fused_w = jnp.concatenate(
        [plane_major(w_gate[0], 0), plane_major(w_up[0], 0), plane_major(router_weight, 0)], axis=1
    )
    down_t = jnp.swapaxes(plane_major(w_down[0], 1), 0, 1)
    contract_first = (((0,), (0,)), ((), ()))
    expert_col = jnp.arange(n_experts, dtype=jnp.int32)[None, :]

    full = lax.all_gather(rows_t, (GX, GY), axis=0, tiled=True)
    fused = lax.dot_general(full, fused_w, contract_first, preferred_element_type=jnp.float32)
    gate = fused[:, :ff_dev]
    upper = fused[:, ff_dev : 2 * ff_dev]
    logits = fused[:, 2 * ff_dev :]
    own_logit = jnp.sum(jnp.where(expert_col == my_expert, logits, 0.0), axis=1)
    other_logit = jnp.sum(jnp.where(expert_col == other_here[:, None], logits, 0.0), axis=1)
    weight = jax.nn.sigmoid(own_logit - other_logit).astype(jnp.bfloat16).astype(jnp.float32)
    hidden = (jax.nn.silu(gate) * upper * weight[:, None]).astype(jnp.bfloat16)
    partial = down_project(down_t, hidden.T)
    summed = lax.psum_scatter(partial, (GX, GY), scatter_dimension=0, tiled=True)

    back = summed.reshape(n_hi, part_width, n_experts, capacity)
    back = jnp.transpose(back, (2, 0, 1, 3)).reshape(n_experts * n_hi, part_width, capacity)
    got = lax.all_to_all(back, (EXPERT, ZH), 0, 0, tiled=True)
    got = got.reshape(n_experts, n_hi, part_width, capacity).astype(jnp.float32)
    returned = jnp.sum(got, axis=1).astype(jnp.bfloat16)
    returned = jnp.swapaxes(returned, 0, 1).reshape(part_width, slots_all)

    combine = dispatch
    mixed = lax.dot_general(combine, returned, (((1,), (1,)), ((), ())), preferred_element_type=jnp.float32)
    return mixed.astype(jnp.bfloat16)


def solution(mesh):
    n_expert, n_tensor = mesh.devices.shape
    fine = Mesh(mesh.devices.reshape(n_expert, 2, 4, n_tensor // 8), (EXPERT, ZH, GX, GY))
    in_specs = (
        P(EXPERT, TENSOR),
        P(),
        P(EXPERT, None),
        P(EXPERT, None, TENSOR),
        P(EXPERT, None, TENSOR),
        P(EXPERT, TENSOR, None),
    )
    out_specs = P(EXPERT, TENSOR)
    return jax.shard_map(body, mesh=fine, in_specs=in_specs, out_specs=out_specs, check_vma=False)
```

```python
import jax
import jax.numpy as jnp
from jax import lax
from jax.experimental import pallas as pl
from jax.sharding import Mesh
from jax.sharding import PartitionSpec as P

EXPERT = "expert"
ZH, GX, GY = "zh", "x", "y"
TENSOR = (ZH, GX, GY)


def _down_kernel(a_ref, b_ref, o_ref):
    o_ref[...] = jnp.dot(a_ref[...], b_ref[...], preferred_element_type=jnp.float32).astype(o_ref.dtype)


def down_project(down_t, hidden_t):
    d_rows, ff = down_t.shape
    rows = hidden_t.shape[1]
    block = 768
    return pl.pallas_call(
        _down_kernel,
        grid=(d_rows // block,),
        in_specs=[pl.BlockSpec((block, ff), lambda i: (i, 0)), pl.BlockSpec((ff, rows), lambda i: (0, 0))],
        out_specs=pl.BlockSpec((block, rows), lambda i: (i, 0)),
        out_shape=jax.ShapeDtypeStruct((d_rows, rows), jnp.bfloat16),
    )(down_t, hidden_t)


def body(tokens, router_weight, expert_ids, w_gate, w_up, w_down):
    tok_rows, part_width = tokens.shape
    top_count = expert_ids.shape[1]
    n_experts = lax.axis_size(EXPERT)
    n_hi = lax.axis_size(ZH)
    n_plane = lax.axis_size(GX) * lax.axis_size(GY)
    capacity = 5 * tok_rows * top_count // (4 * n_experts)
    slots_all = n_experts * capacity
    d_model = router_weight.shape[0]
    my_expert = lax.axis_index(EXPERT)

    flat_ids = expert_ids.reshape(-1)
    picks = tok_rows * top_count
    expert_hot = (flat_ids[:, None] == jnp.arange(n_experts, dtype=jnp.int32)[None, :]).astype(jnp.float32)
    lower = (jnp.arange(picks)[:, None] > jnp.arange(picks)[None, :]).astype(jnp.float32)
    before = jnp.dot(lower, expert_hot, precision=lax.Precision.HIGHEST)
    slot_pos = jnp.sum(before * expert_hot, axis=1).astype(jnp.int32)
    kept = slot_pos < capacity
    target = flat_ids * capacity + slot_pos
    placed = (target[:, None] == jnp.arange(slots_all, dtype=jnp.int32)[None, :]) & kept[:, None]
    placed = placed.reshape(tok_rows, top_count, slots_all).astype(jnp.float32)
    dispatch = jnp.sum(placed, axis=1).astype(jnp.bfloat16)
    other_id = jnp.flip(expert_ids, axis=1).astype(jnp.float32)
    other_of_slot = jnp.sum(placed * other_id[:, :, None], axis=(0, 1))

    bucket_t = lax.dot_general(
        tokens, dispatch, (((0,), (0,)), ((), ())), preferred_element_type=jnp.float32
    ).astype(jnp.bfloat16)
    meta = jnp.broadcast_to(other_of_slot.astype(jnp.bfloat16)[None, :], (8, slots_all))
    payload = jnp.concatenate([bucket_t, meta], axis=0)
    rows_in = payload.shape[0]
    payload = jnp.swapaxes(payload.reshape(rows_in, n_experts, capacity), 0, 1)
    payload = jnp.broadcast_to(payload[:, None], (n_experts, n_hi, rows_in, capacity))
    payload = payload.reshape(n_experts * n_hi, rows_in, capacity)
    got = lax.all_to_all(payload, (EXPERT, ZH), 0, 0, tiled=True)
    got = got.reshape(n_experts, n_hi, rows_in, capacity)
    other_here = got[:, 0, part_width, :].reshape(slots_all).astype(jnp.int32)
    rows_t = jnp.transpose(got[:, :, :part_width, :], (1, 2, 0, 3)).reshape(n_hi * part_width, slots_all)

    def plane_major(w, axis):
        shape = w.shape
        w = w.reshape(shape[:axis] + (n_hi, n_plane, part_width) + shape[axis + 1 :])
        return jnp.swapaxes(w, axis, axis + 1).reshape(shape)

    ff_dev = w_gate.shape[2]
    router_pad = jnp.pad(router_weight, ((0, 0), (0, 128 - n_experts)))
    fused_w = jnp.concatenate(
        [plane_major(w_gate[0], 0), plane_major(w_up[0], 0), plane_major(router_pad, 0)], axis=1
    )
    down_t = jnp.swapaxes(plane_major(w_down[0], 1), 0, 1)
    contract_first = (((0,), (0,)), ((), ()))
    expert_col = jnp.arange(n_experts, dtype=jnp.int32)[None, :]

    full = lax.all_gather(rows_t, (GX, GY), axis=0, tiled=True)
    fused = lax.dot_general(full, fused_w, contract_first, preferred_element_type=jnp.float32)
    gate = fused[:, :ff_dev]
    upper = fused[:, ff_dev : 2 * ff_dev]
    logits = fused[:, 2 * ff_dev : 2 * ff_dev + n_experts]
    own_logit = jnp.sum(jnp.where(expert_col == my_expert, logits, 0.0), axis=1)
    other_logit = jnp.sum(jnp.where(expert_col == other_here[:, None], logits, 0.0), axis=1)
    weight = jax.nn.sigmoid(own_logit - other_logit).astype(jnp.bfloat16).astype(jnp.float32)
    hidden = (jax.nn.silu(gate) * upper * weight[:, None]).astype(jnp.bfloat16)
    partial = down_project(down_t, hidden.T)
    summed = lax.psum_scatter(partial, (GX, GY), scatter_dimension=0, tiled=True)

    back = summed.reshape(n_hi, part_width, n_experts, capacity)
    back = jnp.transpose(back, (2, 0, 1, 3)).reshape(n_experts * n_hi, part_width, capacity)
    got = lax.all_to_all(back, (EXPERT, ZH), 0, 0, tiled=True)
    got = got.reshape(n_experts, n_hi, part_width, capacity).astype(jnp.float32)
    returned = jnp.sum(got, axis=1).astype(jnp.bfloat16)
    returned = jnp.swapaxes(returned, 0, 1).reshape(part_width, slots_all)

    combine = dispatch
    mixed = lax.dot_general(combine, returned, (((1,), (1,)), ((), ())), preferred_element_type=jnp.float32)
    return mixed.astype(jnp.bfloat16)


def solution(mesh):
    n_expert, n_tensor = mesh.devices.shape
    fine = Mesh(mesh.devices.reshape(n_expert, 2, 4, n_tensor // 8), (EXPERT, ZH, GX, GY))
    in_specs = (
        P(EXPERT, TENSOR),
        P(),
        P(EXPERT, None),
        P(EXPERT, None, TENSOR),
        P(EXPERT, None, TENSOR),
        P(EXPERT, TENSOR, None),
    )
    out_specs = P(EXPERT, TENSOR)
    return jax.shard_map(body, mesh=fine, in_specs=in_specs, out_specs=out_specs, check_vma=False)
```

```python
import jax
import jax.numpy as jnp
from jax import lax
from jax.experimental import pallas as pl
from jax.sharding import Mesh
from jax.sharding import PartitionSpec as P

EXPERT = "expert"
ZH, GX, GY = "zh", "x", "y"
TENSOR = (ZH, GX, GY)


def _down_kernel(a_ref, b_ref, o_ref):
    o_ref[...] = jnp.dot(a_ref[...], b_ref[...], preferred_element_type=jnp.float32).astype(o_ref.dtype)


def down_project(down_t, hidden_t):
    d_rows, ff = down_t.shape
    rows = hidden_t.shape[1]
    block = 768
    return pl.pallas_call(
        _down_kernel,
        grid=(d_rows // block,),
        in_specs=[pl.BlockSpec((block, ff), lambda i: (i, 0)), pl.BlockSpec((ff, rows), lambda i: (0, 0))],
        out_specs=pl.BlockSpec((block, rows), lambda i: (i, 0)),
        out_shape=jax.ShapeDtypeStruct((d_rows, rows), jnp.bfloat16),
    )(down_t, hidden_t)


def body(tokens, router_weight, expert_ids, w_gate, w_up, w_down):
    tok_rows, part_width = tokens.shape
    top_count = expert_ids.shape[1]
    n_experts = lax.axis_size(EXPERT)
    n_hi = lax.axis_size(ZH)
    n_plane = lax.axis_size(GX) * lax.axis_size(GY)
    capacity = 5 * tok_rows * top_count // (4 * n_experts)
    slots_all = n_experts * capacity
    d_model = router_weight.shape[0]
    my_expert = lax.axis_index(EXPERT)

    flat_ids = expert_ids.reshape(-1)
    picks = tok_rows * top_count
    expert_hot = (flat_ids[:, None] == jnp.arange(n_experts, dtype=jnp.int32)[None, :]).astype(jnp.float32)
    lower = (jnp.arange(picks)[:, None] > jnp.arange(picks)[None, :]).astype(jnp.float32)
    before = jnp.dot(lower, expert_hot, precision=lax.Precision.HIGHEST)
    slot_pos = jnp.sum(before * expert_hot, axis=1).astype(jnp.int32)
    kept = slot_pos < capacity
    target = flat_ids * capacity + slot_pos
    placed = (target[:, None] == jnp.arange(slots_all, dtype=jnp.int32)[None, :]) & kept[:, None]
    placed = placed.reshape(tok_rows, top_count, slots_all).astype(jnp.float32)
    dispatch = jnp.sum(placed, axis=1).astype(jnp.bfloat16)
    other_id = jnp.flip(expert_ids, axis=1).astype(jnp.float32)
    other_of_slot = jnp.sum(placed * other_id[:, :, None], axis=(0, 1))

    my_hi = lax.axis_index(ZH)
    swap = [(0, 1), (1, 0)]
    partner = lax.ppermute(tokens, ZH, swap)
    first_half = jnp.where(my_hi == 0, tokens, partner)
    second_half = jnp.where(my_hi == 0, partner, tokens)
    tokens_hi = jnp.concatenate([first_half, second_half], axis=1)

    bucket_t = lax.dot_general(
        tokens_hi, dispatch, (((0,), (0,)), ((), ())), preferred_element_type=jnp.float32
    ).astype(jnp.bfloat16)
    meta = jnp.broadcast_to(other_of_slot.astype(jnp.bfloat16)[None, :], (8, slots_all))
    payload = jnp.concatenate([bucket_t, meta], axis=0)
    got = lax.all_to_all(payload, EXPERT, split_axis=1, concat_axis=1, tiled=True)
    rows_t = got[: n_hi * part_width]
    other_here = got[n_hi * part_width].astype(jnp.int32)

    def plane_major(w, axis):
        shape = w.shape
        w = w.reshape(shape[:axis] + (n_hi, n_plane, part_width) + shape[axis + 1 :])
        return jnp.swapaxes(w, axis, axis + 1).reshape(shape)

    ff_dev = w_gate.shape[2]
    router_pad = jnp.pad(router_weight, ((0, 0), (0, 128 - n_experts)))
    fused_w = jnp.concatenate(
        [plane_major(w_gate[0], 0), plane_major(w_up[0], 0), plane_major(router_pad, 0)], axis=1
    )
    down_t = jnp.swapaxes(plane_major(w_down[0], 1), 0, 1)
    contract_first = (((0,), (0,)), ((), ()))
    expert_col = jnp.arange(n_experts, dtype=jnp.int32)[None, :]

    full = lax.all_gather(rows_t, (GX, GY), axis=0, tiled=True)
    fused = lax.dot_general(full, fused_w, contract_first, preferred_element_type=jnp.float32)
    gate = fused[:, :ff_dev]
    upper = fused[:, ff_dev : 2 * ff_dev]
    logits = fused[:, 2 * ff_dev : 2 * ff_dev + n_experts]
    own_logit = jnp.sum(jnp.where(expert_col == my_expert, logits, 0.0), axis=1)
    other_logit = jnp.sum(jnp.where(expert_col == other_here[:, None], logits, 0.0), axis=1)
    weight = jax.nn.sigmoid(own_logit - other_logit).astype(jnp.bfloat16).astype(jnp.float32)
    hidden = (jax.nn.silu(gate) * upper * weight[:, None]).astype(jnp.bfloat16)
    partial = down_project(down_t, hidden.T)
    summed = lax.psum_scatter(partial, (GX, GY), scatter_dimension=0, tiled=True)

    lower_half = summed[:part_width]
    upper_half = summed[part_width:]
    mine = jnp.where(my_hi == 0, lower_half, upper_half)
    theirs = lax.ppermute(jnp.where(my_hi == 0, upper_half, lower_half), ZH, swap)
    total = (mine.astype(jnp.float32) + theirs.astype(jnp.float32)).astype(jnp.bfloat16)
    returned = lax.all_to_all(total, EXPERT, split_axis=1, concat_axis=1, tiled=True)

    combine = dispatch
    mixed = lax.dot_general(combine, returned, (((1,), (1,)), ((), ())), preferred_element_type=jnp.float32)
    return mixed.astype(jnp.bfloat16)


def solution(mesh):
    n_expert, n_tensor = mesh.devices.shape
    fine = Mesh(mesh.devices.reshape(n_expert, 2, 4, n_tensor // 8), (EXPERT, ZH, GX, GY))
    in_specs = (
        P(EXPERT, TENSOR),
        P(),
        P(EXPERT, None),
        P(EXPERT, None, TENSOR),
        P(EXPERT, None, TENSOR),
        P(EXPERT, TENSOR, None),
    )
    out_specs = P(EXPERT, TENSOR)
    return jax.shard_map(body, mesh=fine, in_specs=in_specs, out_specs=out_specs, check_vma=False)
```

```python
import jax
import jax.numpy as jnp
from jax import lax
from jax.experimental import pallas as pl
from jax.sharding import Mesh
from jax.sharding import PartitionSpec as P

EXPERT = "expert"
ZH, GX, GY = "zh", "x", "y"
TENSOR = (ZH, GX, GY)


def _down_kernel(a_ref, b_ref, o_ref):
    o_ref[...] = jnp.dot(a_ref[...], b_ref[...], preferred_element_type=jnp.float32).astype(o_ref.dtype)


def down_project(down_t, hidden_t):
    d_rows, ff = down_t.shape
    rows = hidden_t.shape[1]
    block = 1536
    return pl.pallas_call(
        _down_kernel,
        grid=(d_rows // block,),
        in_specs=[pl.BlockSpec((block, ff), lambda i: (i, 0)), pl.BlockSpec((ff, rows), lambda i: (0, 0))],
        out_specs=pl.BlockSpec((block, rows), lambda i: (i, 0)),
        out_shape=jax.ShapeDtypeStruct((d_rows, rows), jnp.bfloat16),
    )(down_t, hidden_t)


def body(tokens, router_weight, expert_ids, w_gate, w_up, w_down):
    tok_rows, part_width = tokens.shape
    top_count = expert_ids.shape[1]
    n_experts = lax.axis_size(EXPERT)
    n_hi = lax.axis_size(ZH)
    n_plane = lax.axis_size(GX) * lax.axis_size(GY)
    capacity = 5 * tok_rows * top_count // (4 * n_experts)
    slots_all = n_experts * capacity
    d_model = router_weight.shape[0]
    my_expert = lax.axis_index(EXPERT)

    flat_ids = expert_ids.reshape(-1)
    picks = tok_rows * top_count
    expert_hot = (flat_ids[:, None] == jnp.arange(n_experts, dtype=jnp.int32)[None, :]).astype(jnp.float32)
    lower = (jnp.arange(picks)[:, None] > jnp.arange(picks)[None, :]).astype(jnp.float32)
    before = jnp.dot(lower, expert_hot, precision=lax.Precision.HIGHEST)
    slot_pos = jnp.sum(before * expert_hot, axis=1).astype(jnp.int32)
    kept = slot_pos < capacity
    target = flat_ids * capacity + slot_pos
    placed = (target[:, None] == jnp.arange(slots_all, dtype=jnp.int32)[None, :]) & kept[:, None]
    placed = placed.reshape(tok_rows, top_count, slots_all).astype(jnp.float32)
    dispatch = jnp.sum(placed, axis=1).astype(jnp.bfloat16)
    other_id = jnp.flip(expert_ids, axis=1).astype(jnp.float32)
    other_of_slot = jnp.sum(placed * other_id[:, :, None], axis=(0, 1))

    bucket_t = lax.dot_general(
        tokens, dispatch, (((0,), (0,)), ((), ())), preferred_element_type=jnp.float32
    ).astype(jnp.bfloat16)
    meta = jnp.broadcast_to(other_of_slot.astype(jnp.bfloat16)[None, :], (8, slots_all))
    payload = jnp.concatenate([bucket_t, meta], axis=0)
    rows_in = payload.shape[0]
    payload = jnp.swapaxes(payload.reshape(rows_in, n_experts, capacity), 0, 1)
    payload = jnp.broadcast_to(payload[:, None], (n_experts, n_hi, rows_in, capacity))
    payload = payload.reshape(n_experts * n_hi, rows_in, capacity)
    got = lax.all_to_all(payload, (EXPERT, ZH), 0, 0, tiled=True)
    got = got.reshape(n_experts, n_hi, rows_in, capacity)
    other_here = got[:, 0, part_width, :].reshape(slots_all).astype(jnp.int32)
    rows_t = jnp.transpose(got[:, :, :part_width, :], (1, 2, 0, 3)).reshape(n_hi * part_width, slots_all)

    def plane_major(w, axis):
        shape = w.shape
        w = w.reshape(shape[:axis] + (n_hi, n_plane, part_width) + shape[axis + 1 :])
        return jnp.swapaxes(w, axis, axis + 1).reshape(shape)

    ff_dev = w_gate.shape[2]
    router_pad = jnp.pad(router_weight, ((0, 0), (0, 128 - n_experts)))
    fused_w = jnp.concatenate(
        [plane_major(w_gate[0], 0), plane_major(w_up[0], 0), plane_major(router_pad, 0)], axis=1
    )
    down_t = jnp.swapaxes(plane_major(w_down[0], 1), 0, 1)
    contract_first = (((0,), (0,)), ((), ()))
    expert_col = jnp.arange(n_experts, dtype=jnp.int32)[None, :]

    full = lax.all_gather(rows_t, (GX, GY), axis=0, tiled=True)
    fused = lax.dot_general(full, fused_w, contract_first, preferred_element_type=jnp.float32)
    gate = fused[:, :ff_dev]
    upper = fused[:, ff_dev : 2 * ff_dev]
    logits = fused[:, 2 * ff_dev : 2 * ff_dev + n_experts]
    own_logit = jnp.sum(jnp.where(expert_col == my_expert, logits, 0.0), axis=1)
    other_logit = jnp.sum(jnp.where(expert_col == other_here[:, None], logits, 0.0), axis=1)
    weight = jax.nn.sigmoid(own_logit - other_logit).astype(jnp.bfloat16).astype(jnp.float32)
    hidden = (jax.nn.silu(gate) * upper * weight[:, None]).astype(jnp.bfloat16)
    partial = down_project(down_t, hidden.T)
    summed = lax.psum_scatter(partial, (GX, GY), scatter_dimension=0, tiled=True)

    back = summed.reshape(n_hi, part_width, n_experts, capacity)
    back = jnp.transpose(back, (2, 0, 1, 3)).reshape(n_experts * n_hi, part_width, capacity)
    got = lax.all_to_all(back, (EXPERT, ZH), 0, 0, tiled=True)
    got = got.reshape(n_experts, n_hi, part_width, capacity).astype(jnp.float32)
    returned = jnp.sum(got, axis=1).astype(jnp.bfloat16)
    returned = jnp.swapaxes(returned, 0, 1).reshape(part_width, slots_all)

    combine = dispatch
    mixed = lax.dot_general(combine, returned, (((1,), (1,)), ((), ())), preferred_element_type=jnp.float32)
    return mixed.astype(jnp.bfloat16)


def solution(mesh):
    n_expert, n_tensor = mesh.devices.shape
    fine = Mesh(mesh.devices.reshape(n_expert, 2, 4, n_tensor // 8), (EXPERT, ZH, GX, GY))
    in_specs = (
        P(EXPERT, TENSOR),
        P(),
        P(EXPERT, None),
        P(EXPERT, None, TENSOR),
        P(EXPERT, None, TENSOR),
        P(EXPERT, TENSOR, None),
    )
    out_specs = P(EXPERT, TENSOR)
    return jax.shard_map(body, mesh=fine, in_specs=in_specs, out_specs=out_specs, check_vma=False)
```

```python
import jax
import jax.numpy as jnp
from jax import lax
from jax.experimental import pallas as pl
from jax.sharding import Mesh
from jax.sharding import PartitionSpec as P

EXPERT = "expert"
ZH, GX, GY = "zh", "x", "y"
TENSOR = (ZH, GX, GY)


def _down_kernel(a_ref, b_ref, o_ref):
    o_ref[...] = jnp.dot(a_ref[...], b_ref[...], preferred_element_type=jnp.float32).astype(o_ref.dtype)


def down_project(down_t, hidden_t):
    d_rows, ff = down_t.shape
    rows = hidden_t.shape[1]
    block = 3072
    return pl.pallas_call(
        _down_kernel,
        grid=(d_rows // block,),
        in_specs=[pl.BlockSpec((block, ff), lambda i: (i, 0)), pl.BlockSpec((ff, rows), lambda i: (0, 0))],
        out_specs=pl.BlockSpec((block, rows), lambda i: (i, 0)),
        out_shape=jax.ShapeDtypeStruct((d_rows, rows), jnp.bfloat16),
    )(down_t, hidden_t)


def body(tokens, router_weight, expert_ids, w_gate, w_up, w_down):
    tok_rows, part_width = tokens.shape
    top_count = expert_ids.shape[1]
    n_experts = lax.axis_size(EXPERT)
    n_hi = lax.axis_size(ZH)
    n_plane = lax.axis_size(GX) * lax.axis_size(GY)
    capacity = 5 * tok_rows * top_count // (4 * n_experts)
    slots_all = n_experts * capacity
    d_model = router_weight.shape[0]
    my_expert = lax.axis_index(EXPERT)

    flat_ids = expert_ids.reshape(-1)
    picks = tok_rows * top_count
    expert_hot = (flat_ids[:, None] == jnp.arange(n_experts, dtype=jnp.int32)[None, :]).astype(jnp.float32)
    lower = (jnp.arange(picks)[:, None] > jnp.arange(picks)[None, :]).astype(jnp.float32)
    before = jnp.dot(lower, expert_hot, precision=lax.Precision.HIGHEST)
    slot_pos = jnp.sum(before * expert_hot, axis=1).astype(jnp.int32)
    kept = slot_pos < capacity
    target = flat_ids * capacity + slot_pos
    placed = (target[:, None] == jnp.arange(slots_all, dtype=jnp.int32)[None, :]) & kept[:, None]
    placed = placed.reshape(tok_rows, top_count, slots_all).astype(jnp.float32)
    dispatch = jnp.sum(placed, axis=1).astype(jnp.bfloat16)
    other_id = jnp.flip(expert_ids, axis=1).astype(jnp.float32)
    other_of_slot = jnp.sum(placed * other_id[:, :, None], axis=(0, 1))

    bucket_t = lax.dot_general(
        tokens, dispatch, (((0,), (0,)), ((), ())), preferred_element_type=jnp.float32
    ).astype(jnp.bfloat16)
    meta = jnp.broadcast_to(other_of_slot.astype(jnp.bfloat16)[None, :], (8, slots_all))
    payload = jnp.concatenate([bucket_t, meta], axis=0)
    rows_in = payload.shape[0]
    payload = jnp.swapaxes(payload.reshape(rows_in, n_experts, capacity), 0, 1)
    payload = jnp.broadcast_to(payload[:, None], (n_experts, n_hi, rows_in, capacity))
    payload = payload.reshape(n_experts * n_hi, rows_in, capacity)
    got = lax.all_to_all(payload, (EXPERT, ZH), 0, 0, tiled=True)
    got = got.reshape(n_experts, n_hi, rows_in, capacity)
    other_here = got[:, 0, part_width, :].reshape(slots_all).astype(jnp.int32)
    rows_t = jnp.transpose(got[:, :, :part_width, :], (1, 2, 0, 3)).reshape(n_hi * part_width, slots_all)

    def plane_major(w, axis):
        shape = w.shape
        w = w.reshape(shape[:axis] + (n_hi, n_plane, part_width) + shape[axis + 1 :])
        return jnp.swapaxes(w, axis, axis + 1).reshape(shape)

    ff_dev = w_gate.shape[2]
    router_pad = jnp.pad(router_weight, ((0, 0), (0, 128 - n_experts)))
    fused_w = jnp.concatenate(
        [plane_major(w_gate[0], 0), plane_major(w_up[0], 0), plane_major(router_pad, 0)], axis=1
    )
    down_t = jnp.swapaxes(plane_major(w_down[0], 1), 0, 1)
    contract_first = (((0,), (0,)), ((), ()))
    expert_col = jnp.arange(n_experts, dtype=jnp.int32)[None, :]

    full = lax.all_gather(rows_t, (GX, GY), axis=0, tiled=True)
    fused = lax.dot_general(full, fused_w, contract_first, preferred_element_type=jnp.float32)
    gate = fused[:, :ff_dev]
    upper = fused[:, ff_dev : 2 * ff_dev]
    logits = fused[:, 2 * ff_dev : 2 * ff_dev + n_experts]
    own_logit = jnp.sum(jnp.where(expert_col == my_expert, logits, 0.0), axis=1)
    other_logit = jnp.sum(jnp.where(expert_col == other_here[:, None], logits, 0.0), axis=1)
    weight = jax.nn.sigmoid(own_logit - other_logit).astype(jnp.bfloat16).astype(jnp.float32)
    hidden = (jax.nn.silu(gate) * upper * weight[:, None]).astype(jnp.bfloat16)
    partial = down_project(down_t, hidden.T)
    summed = lax.psum_scatter(partial, (GX, GY), scatter_dimension=0, tiled=True)

    back = summed.reshape(n_hi, part_width, n_experts, capacity)
    back = jnp.transpose(back, (2, 0, 1, 3)).reshape(n_experts * n_hi, part_width, capacity)
    got = lax.all_to_all(back, (EXPERT, ZH), 0, 0, tiled=True)
    got = got.reshape(n_experts, n_hi, part_width, capacity).astype(jnp.float32)
    returned = jnp.sum(got, axis=1).astype(jnp.bfloat16)
    returned = jnp.swapaxes(returned, 0, 1).reshape(part_width, slots_all)

    combine = dispatch
    mixed = lax.dot_general(combine, returned, (((1,), (1,)), ((), ())), preferred_element_type=jnp.float32)
    return mixed.astype(jnp.bfloat16)


def solution(mesh):
    n_expert, n_tensor = mesh.devices.shape
    fine = Mesh(mesh.devices.reshape(n_expert, 2, 4, n_tensor // 8), (EXPERT, ZH, GX, GY))
    in_specs = (
        P(EXPERT, TENSOR),
        P(),
        P(EXPERT, None),
        P(EXPERT, None, TENSOR),
        P(EXPERT, None, TENSOR),
        P(EXPERT, TENSOR, None),
    )
    out_specs = P(EXPERT, TENSOR)
    return jax.shard_map(body, mesh=fine, in_specs=in_specs, out_specs=out_specs, check_vma=False)
```

```python
import jax
import jax.numpy as jnp
from jax import lax
from jax.experimental import pallas as pl
from jax.sharding import Mesh
from jax.sharding import PartitionSpec as P

EXPERT = "expert"
ZH, GX, GY = "zh", "x", "y"
TENSOR = (ZH, GX, GY)


def _down_kernel(a_ref, b_ref, o_ref):
    o_ref[...] = jnp.dot(a_ref[...], b_ref[...], preferred_element_type=jnp.float32).astype(o_ref.dtype)


def down_project(down_t, hidden_t):
    d_rows, ff = down_t.shape
    rows = hidden_t.shape[1]
    block = 3072
    return pl.pallas_call(
        _down_kernel,
        grid=(d_rows // block,),
        in_specs=[pl.BlockSpec((block, ff), lambda i: (i, 0)), pl.BlockSpec((ff, rows), lambda i: (0, 0))],
        out_specs=pl.BlockSpec((block, rows), lambda i: (i, 0)),
        out_shape=jax.ShapeDtypeStruct((d_rows, rows), jnp.bfloat16),
    )(down_t, hidden_t)


def body(tokens, router_weight, expert_ids, w_gate, w_up, w_down):
    tok_rows, part_width = tokens.shape
    top_count = expert_ids.shape[1]
    n_experts = lax.axis_size(EXPERT)
    n_hi = lax.axis_size(ZH)
    n_plane = lax.axis_size(GX) * lax.axis_size(GY)
    capacity = 5 * tok_rows * top_count // (4 * n_experts)
    slots_all = n_experts * capacity
    d_model = router_weight.shape[0]
    my_expert = lax.axis_index(EXPERT)

    flat_ids = expert_ids.reshape(-1)
    picks = tok_rows * top_count
    expert_hot = (flat_ids[:, None] == jnp.arange(n_experts, dtype=jnp.int32)[None, :]).astype(jnp.float32)
    lower = (jnp.arange(picks)[:, None] > jnp.arange(picks)[None, :]).astype(jnp.float32)
    before = jnp.dot(lower, expert_hot, precision=lax.Precision.HIGHEST)
    slot_pos = jnp.sum(before * expert_hot, axis=1).astype(jnp.int32)
    kept = slot_pos < capacity
    target = flat_ids * capacity + slot_pos
    placed = (target[:, None] == jnp.arange(slots_all, dtype=jnp.int32)[None, :]) & kept[:, None]
    placed = placed.reshape(tok_rows, top_count, slots_all).astype(jnp.float32)
    dispatch = jnp.sum(placed, axis=1).astype(jnp.bfloat16)
    other_id = jnp.flip(expert_ids, axis=1).astype(jnp.float32)
    other_of_slot = jnp.sum(placed * other_id[:, :, None], axis=(0, 1))

    bucket_t = lax.dot_general(
        tokens, dispatch, (((0,), (0,)), ((), ())), preferred_element_type=jnp.float32
    ).astype(jnp.bfloat16)
    meta = jnp.broadcast_to(other_of_slot.astype(jnp.bfloat16)[None, :], (8, slots_all))
    payload = jnp.concatenate([bucket_t, meta], axis=0)
    rows_in = payload.shape[0]
    payload = jnp.broadcast_to(payload[:, None], (rows_in, n_hi, slots_all)).reshape(rows_in, n_hi * slots_all)
    got = lax.all_to_all(payload, (ZH, EXPERT), 1, 1, tiled=True)
    got = got.reshape(rows_in, n_hi, slots_all)
    other_here = got[part_width, 0].astype(jnp.int32)
    rows_t = got[:part_width].reshape(part_width * n_hi, slots_all)

    def plane_major(w, axis):
        shape = w.shape
        w = w.reshape(shape[:axis] + (n_hi, n_plane, part_width) + shape[axis + 1 :])
        return jnp.swapaxes(w, axis, axis + 1).reshape(shape)

    def feature_minor(w):
        tail = w.shape[1:]
        w = w.reshape((n_hi, n_plane, part_width) + tail)
        return jnp.moveaxis(w, 0, 2).reshape((d_model,) + tail)

    ff_dev = w_gate.shape[2]
    router_pad = jnp.pad(router_weight, ((0, 0), (0, 128 - n_experts)))
    fused_w = jnp.concatenate(
        [feature_minor(w_gate[0]), feature_minor(w_up[0]), feature_minor(router_pad)], axis=1
    )
    down_t = jnp.swapaxes(plane_major(w_down[0], 1), 0, 1)
    contract_first = (((0,), (0,)), ((), ()))
    expert_col = jnp.arange(n_experts, dtype=jnp.int32)[None, :]

    full = lax.all_gather(rows_t, (GX, GY), axis=0, tiled=True)
    fused = lax.dot_general(full, fused_w, contract_first, preferred_element_type=jnp.float32)
    gate = fused[:, :ff_dev]
    upper = fused[:, ff_dev : 2 * ff_dev]
    logits = fused[:, 2 * ff_dev : 2 * ff_dev + n_experts]
    own_logit = jnp.sum(jnp.where(expert_col == my_expert, logits, 0.0), axis=1)
    other_logit = jnp.sum(jnp.where(expert_col == other_here[:, None], logits, 0.0), axis=1)
    weight = jax.nn.sigmoid(own_logit - other_logit).astype(jnp.bfloat16).astype(jnp.float32)
    hidden = (jax.nn.silu(gate) * upper * weight[:, None]).astype(jnp.bfloat16)
    partial = down_project(down_t, hidden.T)
    summed = lax.psum_scatter(partial, (GX, GY), scatter_dimension=0, tiled=True)

    back = summed.reshape(n_hi, part_width, n_experts, capacity)
    back = jnp.transpose(back, (2, 0, 1, 3)).reshape(n_experts * n_hi, part_width, capacity)
    got = lax.all_to_all(back, (EXPERT, ZH), 0, 0, tiled=True)
    got = got.reshape(n_experts, n_hi, part_width, capacity).astype(jnp.float32)
    returned = jnp.sum(got, axis=1).astype(jnp.bfloat16)
    returned = jnp.swapaxes(returned, 0, 1).reshape(part_width, slots_all)

    combine = dispatch
    mixed = lax.dot_general(combine, returned, (((1,), (1,)), ((), ())), preferred_element_type=jnp.float32)
    return mixed.astype(jnp.bfloat16)


def solution(mesh):
    n_expert, n_tensor = mesh.devices.shape
    fine = Mesh(mesh.devices.reshape(n_expert, 2, 4, n_tensor // 8), (EXPERT, ZH, GX, GY))
    in_specs = (
        P(EXPERT, TENSOR),
        P(),
        P(EXPERT, None),
        P(EXPERT, None, TENSOR),
        P(EXPERT, None, TENSOR),
        P(EXPERT, TENSOR, None),
    )
    out_specs = P(EXPERT, TENSOR)
    return jax.shard_map(body, mesh=fine, in_specs=in_specs, out_specs=out_specs, check_vma=False)
```

```python
import jax
import jax.numpy as jnp
from jax import lax
from jax.experimental import pallas as pl
from jax.sharding import Mesh
from jax.sharding import PartitionSpec as P

EXPERT = "expert"
ZH, GX, GY = "zh", "x", "y"
TENSOR = (ZH, GX, GY)


def _down_kernel(a_ref, b_ref, o_ref):
    o_ref[...] = jnp.dot(a_ref[...], b_ref[...], preferred_element_type=jnp.float32).astype(o_ref.dtype)


def down_project(down_t, hidden_t):
    d_rows, ff = down_t.shape
    rows = hidden_t.shape[1]
    block = 3072
    return pl.pallas_call(
        _down_kernel,
        grid=(d_rows // block,),
        in_specs=[pl.BlockSpec((block, ff), lambda i: (i, 0)), pl.BlockSpec((ff, rows), lambda i: (0, 0))],
        out_specs=pl.BlockSpec((block, rows), lambda i: (i, 0)),
        out_shape=jax.ShapeDtypeStruct((d_rows, rows), jnp.bfloat16),
    )(down_t, hidden_t)


def body(tokens, router_weight, expert_ids, w_gate, w_up, w_down):
    tok_rows, part_width = tokens.shape
    top_count = expert_ids.shape[1]
    n_experts = lax.axis_size(EXPERT)
    n_hi = lax.axis_size(ZH)
    n_plane = lax.axis_size(GX) * lax.axis_size(GY)
    capacity = 5 * tok_rows * top_count // (4 * n_experts)
    slots_all = n_experts * capacity
    d_model = router_weight.shape[0]
    my_expert = lax.axis_index(EXPERT)

    flat_ids = expert_ids.reshape(-1)
    picks = tok_rows * top_count
    expert_hot = (flat_ids[:, None] == jnp.arange(n_experts, dtype=jnp.int32)[None, :]).astype(jnp.float32)
    lower = (jnp.arange(picks)[:, None] > jnp.arange(picks)[None, :]).astype(jnp.float32)
    before = jnp.dot(lower, expert_hot, precision=lax.Precision.HIGHEST)
    slot_pos = jnp.sum(before * expert_hot, axis=1).astype(jnp.int32)
    kept = slot_pos < capacity
    target = flat_ids * capacity + slot_pos
    placed = (target[:, None] == jnp.arange(slots_all, dtype=jnp.int32)[None, :]) & kept[:, None]
    placed = placed.reshape(tok_rows, top_count, slots_all).astype(jnp.float32)
    dispatch = jnp.sum(placed, axis=1).astype(jnp.bfloat16)
    other_id = jnp.flip(expert_ids, axis=1).astype(jnp.float32)
    other_of_slot = jnp.sum(placed * other_id[:, :, None], axis=(0, 1))

    bucket_t = lax.dot_general(
        tokens, dispatch, (((0,), (0,)), ((), ())), preferred_element_type=jnp.float32
    ).astype(jnp.bfloat16)
    meta = jnp.broadcast_to(other_of_slot.astype(jnp.bfloat16)[None, :], (8, slots_all))
    payload = jnp.concatenate([bucket_t, meta], axis=0)
    rows_in = payload.shape[0]
    payload = jnp.broadcast_to(payload[:, None], (rows_in, n_hi, slots_all)).reshape(rows_in, n_hi * slots_all)
    got = lax.all_to_all(payload, (ZH, EXPERT), 1, 1, tiled=True)
    got = got.reshape(rows_in, n_hi, slots_all)
    other_here = got[part_width, 0].astype(jnp.int32)
    rows_t = got[:part_width].reshape(part_width * n_hi, slots_all)

    def plane_major(w, axis):
        shape = w.shape
        w = w.reshape(shape[:axis] + (n_hi, n_plane, part_width) + shape[axis + 1 :])
        return jnp.swapaxes(w, axis, axis + 1).reshape(shape)

    def feature_minor(w):
        tail = w.shape[1:]
        w = w.reshape((n_hi, n_plane, part_width) + tail)
        return jnp.moveaxis(w, 0, 2).reshape((d_model,) + tail)

    ff_dev = w_gate.shape[2]
    router_pad = jnp.pad(router_weight, ((0, 0), (0, 128 - n_experts)))
    fused_w = jnp.concatenate(
        [feature_minor(w_gate[0]), feature_minor(w_up[0]), feature_minor(router_pad)], axis=1
    )
    down_t = feature_minor(jnp.swapaxes(w_down[0], 0, 1))
    contract_first = (((0,), (0,)), ((), ()))
    expert_col = jnp.arange(n_experts, dtype=jnp.int32)[None, :]

    full = lax.all_gather(rows_t, (GX, GY), axis=0, tiled=True)
    fused = lax.dot_general(full, fused_w, contract_first, preferred_element_type=jnp.float32)
    gate = fused[:, :ff_dev]
    upper = fused[:, ff_dev : 2 * ff_dev]
    logits = fused[:, 2 * ff_dev : 2 * ff_dev + n_experts]
    own_logit = jnp.sum(jnp.where(expert_col == my_expert, logits, 0.0), axis=1)
    other_logit = jnp.sum(jnp.where(expert_col == other_here[:, None], logits, 0.0), axis=1)
    weight = jax.nn.sigmoid(own_logit - other_logit).astype(jnp.bfloat16).astype(jnp.float32)
    hidden = (jax.nn.silu(gate) * upper * weight[:, None]).astype(jnp.bfloat16)
    partial = down_project(down_t, hidden.T)
    summed = lax.psum_scatter(partial, (GX, GY), scatter_dimension=0, tiled=True)

    back = summed.reshape(part_width, n_hi * slots_all)
    got = lax.all_to_all(back, (ZH, EXPERT), 1, 1, tiled=True)
    got = got.reshape(part_width, n_hi, slots_all).astype(jnp.float32)
    returned = jnp.sum(got, axis=1).astype(jnp.bfloat16)

    combine = dispatch
    mixed = lax.dot_general(combine, returned, (((1,), (1,)), ((), ())), preferred_element_type=jnp.float32)
    return mixed.astype(jnp.bfloat16)


def solution(mesh):
    n_expert, n_tensor = mesh.devices.shape
    fine = Mesh(mesh.devices.reshape(n_expert, 2, 4, n_tensor // 8), (EXPERT, ZH, GX, GY))
    in_specs = (
        P(EXPERT, TENSOR),
        P(),
        P(EXPERT, None),
        P(EXPERT, None, TENSOR),
        P(EXPERT, None, TENSOR),
        P(EXPERT, TENSOR, None),
    )
    out_specs = P(EXPERT, TENSOR)
    return jax.shard_map(body, mesh=fine, in_specs=in_specs, out_specs=out_specs, check_vma=False)
```

```python
import jax
import jax.numpy as jnp
from jax import lax
from jax.experimental import pallas as pl
from jax.sharding import Mesh
from jax.sharding import PartitionSpec as P

EXPERT = "expert"
ZH, GX, GY = "zh", "x", "y"
TENSOR = (ZH, GX, GY)


def _down_kernel(a_ref, b_ref, o_ref):
    o_ref[...] = jnp.dot(a_ref[...], b_ref[...], preferred_element_type=jnp.float32).astype(o_ref.dtype)


def down_project(down_t, hidden_t):
    d_rows, ff = down_t.shape
    rows = hidden_t.shape[1]
    block = 3072
    return pl.pallas_call(
        _down_kernel,
        grid=(d_rows // block,),
        in_specs=[pl.BlockSpec((block, ff), lambda i: (i, 0)), pl.BlockSpec((ff, rows), lambda i: (0, 0))],
        out_specs=pl.BlockSpec((block, rows), lambda i: (i, 0)),
        out_shape=jax.ShapeDtypeStruct((d_rows, rows), jnp.bfloat16),
    )(down_t, hidden_t)


def body(tokens, router_weight, expert_ids, w_gate, w_up, w_down):
    tok_rows, part_width = tokens.shape
    top_count = expert_ids.shape[1]
    n_experts = lax.axis_size(EXPERT)
    n_hi = lax.axis_size(ZH)
    n_plane = lax.axis_size(GX) * lax.axis_size(GY)
    capacity = 5 * tok_rows * top_count // (4 * n_experts)
    slots_all = n_experts * capacity
    d_model = router_weight.shape[0]
    my_expert = lax.axis_index(EXPERT)

    flat_ids = expert_ids.reshape(-1)
    picks = tok_rows * top_count
    expert_hot = (flat_ids[:, None] == jnp.arange(n_experts, dtype=jnp.int32)[None, :]).astype(jnp.float32)
    lower = (jnp.arange(picks)[:, None] > jnp.arange(picks)[None, :]).astype(jnp.float32)
    before = jnp.dot(lower, expert_hot, precision=lax.Precision.HIGHEST)
    slot_pos = jnp.sum(before * expert_hot, axis=1).astype(jnp.int32)
    kept = slot_pos < capacity
    target = flat_ids * capacity + slot_pos
    placed = (target[:, None] == jnp.arange(slots_all, dtype=jnp.int32)[None, :]) & kept[:, None]
    placed = placed.reshape(tok_rows, top_count, slots_all).astype(jnp.float32)
    dispatch = jnp.sum(placed, axis=1).astype(jnp.bfloat16)
    other_id = jnp.flip(expert_ids, axis=1).astype(jnp.float32)
    other_of_slot = jnp.sum(placed * other_id[:, :, None], axis=(0, 1))

    bucket_t = lax.dot_general(
        tokens, dispatch, (((0,), (0,)), ((), ())), preferred_element_type=jnp.float32
    ).astype(jnp.bfloat16)
    meta = jnp.broadcast_to(other_of_slot.astype(jnp.bfloat16)[None, :], (8, slots_all))
    payload = jnp.concatenate([bucket_t, meta], axis=0)
    rows_in = payload.shape[0]
    payload = jnp.broadcast_to(payload[:, None], (rows_in, n_hi, slots_all)).reshape(rows_in, n_hi * slots_all)
    got = lax.all_to_all(payload, (ZH, EXPERT), 1, 1, tiled=True)
    got = got.reshape(rows_in, n_hi, slots_all)
    other_here = got[part_width, 0].astype(jnp.int32)
    rows_t = got[:part_width].reshape(part_width * n_hi, slots_all)

    def plane_major(w, axis):
        shape = w.shape
        w = w.reshape(shape[:axis] + (n_hi, n_plane, part_width) + shape[axis + 1 :])
        return jnp.swapaxes(w, axis, axis + 1).reshape(shape)

    def feature_minor(w):
        tail = w.shape[1:]
        w = w.reshape((n_hi, n_plane, part_width) + tail)
        return jnp.moveaxis(w, 0, 2).reshape((d_model,) + tail)

    ff_dev = w_gate.shape[2]
    fused_w = jnp.concatenate(
        [feature_minor(w_gate[0]), feature_minor(w_up[0]), feature_minor(router_weight)], axis=1
    )
    down_t = jnp.swapaxes(plane_major(w_down[0], 1), 0, 1)
    contract_first = (((0,), (0,)), ((), ()))
    expert_col = jnp.arange(n_experts, dtype=jnp.int32)[None, :]

    full = lax.all_gather(rows_t, (GX, GY), axis=0, tiled=True)
    fused = lax.dot_general(full, fused_w, contract_first, preferred_element_type=jnp.float32)
    gate = fused[:, :ff_dev]
    upper = fused[:, ff_dev : 2 * ff_dev]
    logits = fused[:, 2 * ff_dev : 2 * ff_dev + n_experts]
    own_logit = jnp.sum(jnp.where(expert_col == my_expert, logits, 0.0), axis=1)
    other_logit = jnp.sum(jnp.where(expert_col == other_here[:, None], logits, 0.0), axis=1)
    weight = jax.nn.sigmoid(own_logit - other_logit).astype(jnp.bfloat16).astype(jnp.float32)
    hidden = (jax.nn.silu(gate) * upper * weight[:, None]).astype(jnp.bfloat16)
    partial = down_project(down_t, hidden.T)
    summed = lax.psum_scatter(partial, (GX, GY), scatter_dimension=0, tiled=True)

    back = summed.reshape(n_hi, part_width, n_experts, capacity)
    back = jnp.transpose(back, (2, 0, 1, 3)).reshape(n_experts * n_hi, part_width, capacity)
    got = lax.all_to_all(back, (EXPERT, ZH), 0, 0, tiled=True)
    got = got.reshape(n_experts, n_hi, part_width, capacity).astype(jnp.float32)
    returned = jnp.sum(got, axis=1).astype(jnp.bfloat16)
    returned = jnp.swapaxes(returned, 0, 1).reshape(part_width, slots_all)

    combine = dispatch
    mixed = lax.dot_general(combine, returned, (((1,), (1,)), ((), ())), preferred_element_type=jnp.float32)
    return mixed.astype(jnp.bfloat16)


def solution(mesh):
    n_expert, n_tensor = mesh.devices.shape
    fine = Mesh(mesh.devices.reshape(n_expert, 2, 4, n_tensor // 8), (EXPERT, ZH, GX, GY))
    in_specs = (
        P(EXPERT, TENSOR),
        P(),
        P(EXPERT, None),
        P(EXPERT, None, TENSOR),
        P(EXPERT, None, TENSOR),
        P(EXPERT, TENSOR, None),
    )
    out_specs = P(EXPERT, TENSOR)
    return jax.shard_map(body, mesh=fine, in_specs=in_specs, out_specs=out_specs, check_vma=False)
```
